512 devices in a mesh: grp: 16 (over x_lo, z), seq: 32 (over y, x_hi, core).
Axes of the slice: x: 4 (x_hi: 2, x_lo: 2; x = x_hi * 2 + x_lo), y: 8, z: 8, core: 2. Of those that a mesh axis runs over, the one named last changes fastest.
Arguments:
- signal: bfloat16 [131072, 256], P(('grp', 'seq')), may hold values from -6 to 6
- cotangent: bfloat16 [131072, 256], P(('grp', 'seq')), may hold values from -6 to 6
- w_taps: bfloat16 [512, 1024], replicated, may hold values from -0.25 to 0.25
- gate_bias: float32 [1024], replicated, may hold values from -3 to 3
- w_out: bfloat16 [512, 256], replicated, may hold values from -0.25 to 0.25
Outputs:
- block_out: bfloat16 [131072, 256], P(('grp', 'seq'))
- grad_in: bfloat16 [131072, 256], P(('grp', 'seq'))
- grad_taps: float32 [512, 1024], P('seq')
- grad_bias: float32 [1024], P('seq')
- grad_out: float32 [512, 256], P('seq')
The draws below stay inside these ranges and needn't reach their ends.
All inputs are finite; a program needn't handle non-finite values.
Results may differ from the reference program's by a relative error of at most 0.0045.
Values may be sent and summed in bfloat16 or wider, within the bound.
No kernel may reach another device: no remote copies, remote signals or barrier semaphores. Data moves between devices by JAX's collectives and lax.ppermute only.
A program may use at most 64 MiB of HBM per device.

```python
import jax
import jax.numpy as jnp
from jax import lax

CHANNEL_COUNT = 256
H = 512
TS = 256
DILATION_GAP = 512
TIME_STEPS = 131072


def block_levels(stream_key, dims, cuts, smallest, largest):
    factor_of, own = 1.0, jax.random.fold_in(stream_key, 6)
    for position, parts in cuts:
        steps = jnp.exp(jax.random.uniform(jax.random.fold_in(own, position), (parts,), jnp.float32, smallest / len(cuts), largest / len(cuts)))
        factor_of = factor_of * jnp.repeat(steps, dims[position] // parts).reshape([-1 if axis == position else 1 for axis in range(len(dims))])
    return factor_of


def normal_values(rng, extent, spread, bound, cuts=(), dtype=jnp.bfloat16):
    factor_of = block_levels(rng, extent, cuts, -0.22, 0.18) if cuts else 1.0
    entries = jax.random.normal(rng, extent, jnp.float32) * spread * factor_of
    return jnp.minimum(jnp.maximum(entries, -bound), bound).astype(dtype)


def setup_inputs(seed: int = 0) -> dict:
    streams_of = jax.random.split(jax.random.key(seed), 6)
    signal = normal_values(streams_of[0], (TIME_STEPS, CHANNEL_COUNT), 1.0, 6.0, ((0, 512),))
    cotangent = normal_values(streams_of[1], (TIME_STEPS, CHANNEL_COUNT), 1.0, 6.0, ((0, 512),))
    w_taps = normal_values(streams_of[2], (2 * CHANNEL_COUNT, 2 * H), (2 * CHANNEL_COUNT) ** -0.5, 0.25)
    gate_bias = normal_values(streams_of[3], (2 * H,), 0.5, 3.0, (), jnp.float32)
    w_out = normal_values(streams_of[4], (H, CHANNEL_COUNT), H ** -0.5, 0.25)
    return dict(signal=signal, cotangent=cotangent, w_taps=w_taps, gate_bias=gate_bias, w_out=w_out)


def reduced_row_axes(left, right):
    return lax.dot_general(left, right, (((0,), (0,)), ((), ())), preferred_element_type=jnp.float32)


def contract_cols(left, right):
    return lax.dot_general(left, right, (((1,), (1,)), ((), ())), preferred_element_type=jnp.float32)


def reference(signal, cotangent, w_taps, gate_bias, w_out):
    span = TS * 8
    blocks = TIME_STEPS // span
    lagged_input = jnp.concatenate([jnp.zeros((DILATION_GAP, CHANNEL_COUNT), jnp.bfloat16), signal[:TIME_STEPS - DILATION_GAP]], axis=0)

    def step(carry, items):
        grad_taps, grad_bias, grad_out = carry
        rows, delay_rows, cot_rows = items
        inputs = jnp.concatenate([delay_rows, rows], axis=1)
        preact = jnp.dot(inputs, w_taps, preferred_element_type=jnp.float32) + gate_bias
        squashed = jnp.tanh(preact[:, :H])
        opened = jax.nn.sigmoid(preact[:, H:])
        hidden_state = (squashed * opened).astype(jnp.bfloat16)
        output = (rows.astype(jnp.float32) + jnp.dot(hidden_state, w_out, preferred_element_type=jnp.float32)).astype(jnp.bfloat16)
        grad_hidden = contract_cols(cot_rows, w_out)
        grad_pre = jnp.concatenate([grad_hidden * opened * (1.0 - squashed * squashed),
                                    grad_hidden * squashed * opened * (1.0 - opened)], axis=1).astype(jnp.bfloat16)
        grad_out = grad_out + reduced_row_axes(hidden_state, cot_rows)
        grad_taps = grad_taps + reduced_row_axes(inputs, grad_pre)
        grad_bias = grad_bias + jnp.sum(grad_pre.astype(jnp.float32), axis=0)
        back = contract_cols(grad_pre, w_taps)
        nearby = cot_rows.astype(jnp.float32) + back[:, CHANNEL_COUNT:]
        return (grad_taps, grad_bias, grad_out), (output, nearby, back[:, :CHANNEL_COUNT])

    init = (jnp.zeros((2 * CHANNEL_COUNT, 2 * H), jnp.float32), jnp.zeros((2 * H,), jnp.float32), jnp.zeros((H, CHANNEL_COUNT), jnp.float32))
    items = (signal.reshape(blocks, span, CHANNEL_COUNT), lagged_input.reshape(blocks, span, CHANNEL_COUNT), cotangent.reshape(blocks, span, CHANNEL_COUNT))
    sums, outs = lax.scan(step, init, items)
    grad_taps, grad_bias, grad_out = sums
    block_out = outs[0].reshape(TIME_STEPS, CHANNEL_COUNT)
    nearby = outs[1].reshape(TIME_STEPS, CHANNEL_COUNT)
    tapped_signal = outs[2].reshape(TIME_STEPS, CHANNEL_COUNT)
    future_part = jnp.concatenate([tapped_signal[DILATION_GAP:], jnp.zeros((DILATION_GAP, CHANNEL_COUNT), jnp.float32)], axis=0)
    grad_in = (nearby + future_part).astype(jnp.bfloat16)
    return (block_out, grad_in, grad_taps, grad_bias, grad_out)
```

```python
import jax
import jax.numpy as jnp
from jax import lax
from jax.sharding import PartitionSpec as P


def from_behind(array, axis, by):
    count = lax.axis_size(axis)
    pairs = [(i, i + by) for i in range(count) if 0 <= i + by < count]
    return lax.ppermute(array, axis, pairs)


def reduced_row_axes(left, right):
    return lax.dot_general(
        left, right, (((0,), (0,)), ((), ())), preferred_element_type=jnp.float32
    )


def contract_cols(left, right):
    return lax.dot_general(
        left, right, (((1,), (1,)), ((), ())), preferred_element_type=jnp.float32
    )


def per_device(signal, cotangent, w_taps, gate_bias, w_out):
    width = signal.shape[1]
    units = w_out.shape[0]
    lagged_input = from_behind(signal, ("grp", "seq"), 2)
    preact = jnp.dot(signal, w_taps[width:], preferred_element_type=jnp.float32)
    preact = (
        preact
        + jnp.dot(lagged_input, w_taps[:width], preferred_element_type=jnp.float32)
        + gate_bias
    )
    squashed = jnp.tanh(preact[:, :units])
    opened = jax.nn.sigmoid(preact[:, units:])
    hidden_state = (squashed * opened).astype(jnp.bfloat16)
    block_out = (
        signal.astype(jnp.float32)
        + jnp.dot(hidden_state, w_out, preferred_element_type=jnp.float32)
    ).astype(jnp.bfloat16)
    grad_hidden = contract_cols(cotangent, w_out)
    grad_pre = jnp.concatenate(
        [
            grad_hidden * opened * (1.0 - squashed * squashed),
            grad_hidden * squashed * opened * (1.0 - opened),
        ],
        axis=1,
    ).astype(jnp.bfloat16)
    part_out = reduced_row_axes(hidden_state, cotangent)
    part_taps = jnp.concatenate(
        [reduced_row_axes(lagged_input, grad_pre), reduced_row_axes(signal, grad_pre)], axis=0
    )
    part_bias = jnp.sum(grad_pre.astype(jnp.float32), axis=0)
    later_pre = from_behind(grad_pre, ("grp", "seq"), -2)
    tapped_signal = contract_cols(later_pre, w_taps[:width])
    nearby = cotangent.astype(jnp.float32) + contract_cols(grad_pre, w_taps[width:])
    grad_in = (nearby + tapped_signal).astype(jnp.bfloat16)
    groups = lax.axis_size("seq")
    lanes = 128
    rows_taps = part_taps.shape[0] // groups
    rows_out = part_out.shape[0] // groups
    share_bias = part_bias.shape[0] // groups
    taps_r = rows_taps * part_taps.shape[1] // lanes
    out_r = rows_out * part_out.shape[1] // lanes
    bias_r = 8
    bias_rows = jnp.pad(part_bias.reshape(groups, 1, share_bias), ((0, 0), (0, bias_r), (0, lanes - share_bias)))[:, :bias_r]
    packed = jnp.concatenate(
        [
            part_taps.reshape(groups, taps_r, lanes),
            part_out.reshape(groups, out_r, lanes),
            bias_rows,
        ],
        axis=1,
    ).reshape(groups * (taps_r + out_r + bias_r), lanes)
    mine = lax.psum_scatter(packed, "seq", scatter_dimension=0, tiled=True)
    mine = lax.psum(mine, "grp")
    grad_taps = mine[:taps_r].reshape(rows_taps, part_taps.shape[1])
    grad_out = mine[taps_r : taps_r + out_r].reshape(rows_out, part_out.shape[1])
    grad_bias = mine[taps_r + out_r, :share_bias]
    return (block_out, grad_in, grad_taps, grad_bias, grad_out)


def solution(mesh):
    placed = (P(("grp", "seq"), None), P(("grp", "seq"), None), P(), P(), P())
    return jax.shard_map(
        per_device,
        mesh=mesh,
        in_specs=placed,
        out_specs=(
            P(("grp", "seq"), None),
            P(("grp", "seq"), None),
            P("seq", None),
            P("seq"),
            P("seq", None),
        ),
        check_vma=False,
    )
```

```python
import jax
import jax.numpy as jnp
from jax import lax
from jax.sharding import PartitionSpec as P


def from_behind(array, axis, by):
    count = lax.axis_size(axis)
    pairs = [(i, i + by) for i in range(count) if 0 <= i + by < count]
    return lax.ppermute(array, axis, pairs)


def reduced_row_axes(left, right):
    return lax.dot_general(
        left, right, (((0,), (0,)), ((), ())), preferred_element_type=jnp.float32
    )


def contract_cols(left, right):
    return lax.dot_general(
        left, right, (((1,), (1,)), ((), ())), preferred_element_type=jnp.float32
    )


def exchange(array, axis, mask):
    count = lax.axis_size(axis)
    return lax.ppermute(array, axis, [(i, i ^ mask) for i in range(count)])


def bit_order(count):
    bits = count.bit_length() - 1
    order = [0] + list(range(2, bits)) + [1] if bits > 2 else list(range(bits))
    if bits == 5:
        order = [0, 2, 3, 1, 4]
    return order


def halving_scatter(shares, axis):
    count = shares.shape[0]
    bits = count.bit_length() - 1
    order = bit_order(count)
    rest = shares.shape[1:]
    shaped = shares.reshape((2,) * bits + rest)
    shaped = jnp.transpose(
        shaped, [bits - 1 - b for b in order] + list(range(bits, bits + len(rest)))
    )
    buf = shaped.reshape((count,) + rest)
    where = lax.axis_index(axis)
    for b in order:
        mask = 1 << b
        bit = (where >> b) & 1
        halves = buf.reshape((2, buf.shape[0] // 2) + rest)
        keep = lax.dynamic_index_in_dim(halves, bit, 0, keepdims=False)
        send = lax.dynamic_index_in_dim(halves, 1 - bit, 0, keepdims=False)
        buf = keep + exchange(send, axis, mask)
    return buf[0]


def butterfly_sum(array, axis):
    count = lax.axis_size(axis)
    bits = count.bit_length() - 1
    order = [0, bits - 1] + list(range(1, bits - 1)) if bits > 1 else list(range(bits))
    for b in order:
        array = array + exchange(array, axis, 1 << b)
    return array


def per_device(signal, cotangent, w_taps, gate_bias, w_out):
    width = signal.shape[1]
    units = w_out.shape[0]
    lagged_input = from_behind(signal, ("grp", "seq"), 2)
    preact = jnp.dot(signal, w_taps[width:], preferred_element_type=jnp.float32)
    preact = (
        preact
        + jnp.dot(lagged_input, w_taps[:width], preferred_element_type=jnp.float32)
        + gate_bias
    )
    squashed = jnp.tanh(preact[:, :units])
    opened = jax.nn.sigmoid(preact[:, units:])
    hidden_state = (squashed * opened).astype(jnp.bfloat16)
    block_out = (
        signal.astype(jnp.float32)
        + jnp.dot(hidden_state, w_out, preferred_element_type=jnp.float32)
    ).astype(jnp.bfloat16)
    grad_hidden = contract_cols(cotangent, w_out)
    grad_pre = jnp.concatenate(
        [
            grad_hidden * opened * (1.0 - squashed * squashed),
            grad_hidden * squashed * opened * (1.0 - opened),
        ],
        axis=1,
    ).astype(jnp.bfloat16)
    part_out = reduced_row_axes(hidden_state, cotangent)
    part_taps = jnp.concatenate(
        [reduced_row_axes(lagged_input, grad_pre), reduced_row_axes(signal, grad_pre)], axis=0
    )
    part_bias = jnp.sum(grad_pre.astype(jnp.float32), axis=0)
    later_pre = from_behind(grad_pre, ("grp", "seq"), -2)
    tapped_signal = contract_cols(later_pre, w_taps[:width])
    nearby = cotangent.astype(jnp.float32) + contract_cols(grad_pre, w_taps[width:])
    grad_in = (nearby + tapped_signal).astype(jnp.bfloat16)
    groups = lax.axis_size("seq")
    lanes = 128
    rows_taps = part_taps.shape[0] // groups
    rows_out = part_out.shape[0] // groups
    share_bias = part_bias.shape[0] // groups
    taps_r = rows_taps * part_taps.shape[1] // lanes
    out_r = rows_out * part_out.shape[1] // lanes
    bias_r = 8
    bias_rows = jnp.pad(part_bias.reshape(groups, 1, share_bias), ((0, 0), (0, bias_r), (0, lanes - share_bias)))[:, :bias_r]
    packed = jnp.concatenate(
        [
            part_taps.reshape(groups, taps_r, lanes),
            part_out.reshape(groups, out_r, lanes),
            bias_rows,
        ],
        axis=1,
    )
    mine = halving_scatter(packed, "seq")
    mine = butterfly_sum(mine, "grp")
    grad_taps = mine[:taps_r].reshape(rows_taps, part_taps.shape[1])
    grad_out = mine[taps_r : taps_r + out_r].reshape(rows_out, part_out.shape[1])
    grad_bias = mine[taps_r + out_r, :share_bias]
    return (block_out, grad_in, grad_taps, grad_bias, grad_out)


def solution(mesh):
    placed = (P(("grp", "seq"), None), P(("grp", "seq"), None), P(), P(), P())
    return jax.shard_map(
        per_device,
        mesh=mesh,
        in_specs=placed,
        out_specs=(
            P(("grp", "seq"), None),
            P(("grp", "seq"), None),
            P("seq", None),
            P("seq"),
            P("seq", None),
        ),
        check_vma=False,
    )
```

```python
import jax
import jax.numpy as jnp
from jax import lax
from jax.sharding import PartitionSpec as P


def from_behind(array, axis, by):
    count = lax.axis_size(axis)
    pairs = [(i, i + by) for i in range(count) if 0 <= i + by < count]
    return lax.ppermute(array, axis, pairs)


def reduced_row_axes(left, right):
    return lax.dot_general(
        left, right, (((0,), (0,)), ((), ())), preferred_element_type=jnp.float32
    )


def contract_cols(left, right):
    return lax.dot_general(
        left, right, (((1,), (1,)), ((), ())), preferred_element_type=jnp.float32
    )


def exchange(array, axes, mask):
    count = lax.axis_size(axes)
    return lax.ppermute(array, axes, [(i, i ^ mask) for i in range(count)])


def chain_layout(order, home):
    bits = len(order)
    return [bits - 1 - home[b] for b in order]


def halving_scatter(packed, axes, orders, widths, home):
    bits = len(orders[0])
    count = packed.shape[0]
    where = lax.axis_index(axes)
    bufs = []
    col = 0
    for order, width in zip(orders, widths):
        part = packed[:, col : col + width].reshape((2,) * bits + (width,))
        part = jnp.transpose(part, chain_layout(order, home) + [bits])
        bufs.append(part.reshape(count, width))
        col += width
    for step in range(bits):
        keeps, sends = [], []
        for i, order in enumerate(orders):
            bit = (where >> order[step]) & 1
            buf = bufs[i]
            halves = buf.reshape((2, buf.shape[0] // 2, buf.shape[1]))
            keeps.append(lax.dynamic_index_in_dim(halves, bit, 0, keepdims=False))
            sends.append(lax.dynamic_index_in_dim(halves, 1 - bit, 0, keepdims=False))
        sends = lax.optimization_barrier(sends)
        got = [exchange(send, axes, 1 << order[step]) for send, order in zip(sends, orders)]
        got = lax.optimization_barrier(got)
        bufs = [keep + recv for keep, recv in zip(keeps, got)]
    return jnp.concatenate(bufs, axis=1)


def doubling_gather(piece, axes, bits):
    where = lax.axis_index(axes)
    for b in bits:
        got = exchange(piece, axes, 1 << b)
        upper = ((where >> b) & 1) == 1
        piece = jnp.where(upper, jnp.concatenate([got, piece]), jnp.concatenate([piece, got]))
    return piece


def per_device(signal, cotangent, w_taps, gate_bias, w_out):
    width = signal.shape[1]
    units = w_out.shape[0]
    lagged_input = from_behind(signal, ("grp", "seq"), 2)
    preact = jnp.dot(signal, w_taps[width:], preferred_element_type=jnp.float32)
    preact = (
        preact
        + jnp.dot(lagged_input, w_taps[:width], preferred_element_type=jnp.float32)
        + gate_bias
    )
    squashed = jnp.tanh(preact[:, :units])
    opened = jax.nn.sigmoid(preact[:, units:])
    hidden_state = (squashed * opened).astype(jnp.bfloat16)
    block_out = (
        signal.astype(jnp.float32)
        + jnp.dot(hidden_state, w_out, preferred_element_type=jnp.float32)
    ).astype(jnp.bfloat16)
    grad_hidden = contract_cols(cotangent, w_out)
    grad_pre = jnp.concatenate(
        [
            grad_hidden * opened * (1.0 - squashed * squashed),
            grad_hidden * squashed * opened * (1.0 - opened),
        ],
        axis=1,
    ).astype(jnp.bfloat16)
    part_out = reduced_row_axes(hidden_state, cotangent)
    part_taps = jnp.concatenate(
        [reduced_row_axes(lagged_input, grad_pre), reduced_row_axes(signal, grad_pre)], axis=0
    )
    part_bias = jnp.sum(grad_pre.astype(jnp.float32), axis=0)
    later_pre = from_behind(grad_pre, ("grp", "seq"), -2)
    tapped_signal = contract_cols(later_pre, w_taps[:width])
    nearby = cotangent.astype(jnp.float32) + contract_cols(grad_pre, w_taps[width:])
    grad_in = (nearby + tapped_signal).astype(jnp.bfloat16)
    seq_n = lax.axis_size("seq")
    grp_n = lax.axis_size("grp")
    chunks = seq_n * grp_n
    pair = part_bias.shape[0] // chunks
    used = part_taps.shape[1] + part_out.shape[1] + pair
    lanes = 128
    width = -(-used // lanes) * lanes
    packed = jnp.concatenate(
        [
            part_taps.reshape(chunks, -1),
            part_out.reshape(chunks, -1),
            part_bias.reshape(chunks, pair),
            jnp.zeros((chunks, width - used), jnp.float32),
        ],
        axis=1,
    )
    seq_bits = seq_n.bit_length() - 1
    grp_bits = grp_n.bit_length() - 1
    home = {}
    for b in range(seq_bits + grp_bits):
        home[b] = b + grp_bits if b < seq_bits else b - seq_bits
    core, x_hi, y1, y2, y4 = 0, 1, 2, 3, 4
    z1, z2, z4, x_lo = 5, 6, 7, 8
    orders = (
        [core, y1, z1, x_lo, y2, z2, x_hi, y4, z4],
        [core, z1, x_lo, y1, z2, x_hi, y2, z4, y4],
        [core, x_lo, y1, z1, x_hi, y2, z2, y4, z4],
    )
    lanes_per = width // lanes
    split = [lanes_per // 3 + (1 if i < lanes_per % 3 else 0) for i in range(3)]
    widths = [n * lanes for n in split]
    mine = halving_scatter(packed, ("grp", "seq"), orders, widths, home)
    share = doubling_gather(mine, ("grp", "seq"), [z1, z2, z4, x_lo])
    taps_w = part_taps.shape[1]
    out_w = part_out.shape[1]
    grad_taps = share[:, :taps_w]
    grad_out = share[:, taps_w : taps_w + out_w]
    grad_bias = share[:, taps_w + out_w : used].reshape(-1)
    return (block_out, grad_in, grad_taps, grad_bias, grad_out)


def solution(mesh):
    placed = (P(("grp", "seq"), None), P(("grp", "seq"), None), P(), P(), P())
    return jax.shard_map(
        per_device,
        mesh=mesh,
        in_specs=placed,
        out_specs=(
            P(("grp", "seq"), None),
            P(("grp", "seq"), None),
            P("seq", None),
            P("seq"),
            P("seq", None),
        ),
        check_vma=False,
    )
```

```python
import jax
import jax.numpy as jnp
from jax import lax
from jax.sharding import PartitionSpec as P


def from_behind(array, axis, by):
    count = lax.axis_size(axis)
    pairs = [(i, i + by) for i in range(count) if 0 <= i + by < count]
    return lax.ppermute(array, axis, pairs)


def reduced_row_axes(left, right):
    return lax.dot_general(
        left, right, (((0,), (0,)), ((), ())), preferred_element_type=jnp.float32
    )


def contract_cols(left, right):
    return lax.dot_general(
        left, right, (((1,), (1,)), ((), ())), preferred_element_type=jnp.float32
    )


def exchange(array, axes, mask):
    count = lax.axis_size(axes)
    return lax.ppermute(array, axes, [(i, i ^ mask) for i in range(count)])


def chain_layout(order, home):
    bits = len(order)
    return [bits - 1 - home[b] for b in order]


def halving_scatter(packed, axes, orders, home):
    bits = len(orders[0])
    count, width = packed.shape
    lead = orders[0][0]
    where = lax.axis_index(axes)
    natural = packed.reshape((2,) * bits + (width,))
    halves = []
    for k, order in enumerate(orders):
        part = jnp.transpose(natural, chain_layout(order, home) + [bits])[k]
        halves.append(part.reshape(count // 2, width))
    buf = jnp.concatenate(halves)
    first = (where >> lead) & 1
    for step in range(bits):
        shift = [order[step] for order in orders]
        bit = jnp.where(first == 0, (where >> shift[0]) & 1, (where >> shift[1]) & 1)
        pairs = [(i, i ^ (1 << shift[(i >> lead) & 1])) for i in range(count)]
        split = buf.reshape((2, buf.shape[0] // 2, width))
        keep = lax.dynamic_index_in_dim(split, bit, 0, keepdims=False)
        send = lax.dynamic_index_in_dim(split, 1 - bit, 0, keepdims=False)
        buf = keep + lax.ppermute(send, axes, pairs)
    return buf


def doubling_gather(piece, axes, bits):
    where = lax.axis_index(axes)
    for b in bits:
        got = exchange(piece, axes, 1 << b)
        upper = ((where >> b) & 1) == 1
        piece = jnp.where(upper, jnp.concatenate([got, piece]), jnp.concatenate([piece, got]))
    return piece


def per_device(signal, cotangent, w_taps, gate_bias, w_out):
    width = signal.shape[1]
    units = w_out.shape[0]
    lagged_input = from_behind(signal, ("grp", "seq"), 2)
    preact = jnp.dot(signal, w_taps[width:], preferred_element_type=jnp.float32)
    preact = (
        preact
        + jnp.dot(lagged_input, w_taps[:width], preferred_element_type=jnp.float32)
        + gate_bias
    )
    squashed = jnp.tanh(preact[:, :units])
    opened = jax.nn.sigmoid(preact[:, units:])
    hidden_state = (squashed * opened).astype(jnp.bfloat16)
    block_out = (
        signal.astype(jnp.float32)
        + jnp.dot(hidden_state, w_out, preferred_element_type=jnp.float32)
    ).astype(jnp.bfloat16)
    grad_hidden = contract_cols(cotangent, w_out)
    grad_pre = jnp.concatenate(
        [
            grad_hidden * opened * (1.0 - squashed * squashed),
            grad_hidden * squashed * opened * (1.0 - opened),
        ],
        axis=1,
    ).astype(jnp.bfloat16)
    part_out = reduced_row_axes(hidden_state, cotangent)
    part_taps = jnp.concatenate(
        [reduced_row_axes(lagged_input, grad_pre), reduced_row_axes(signal, grad_pre)], axis=0
    )
    part_bias = jnp.sum(grad_pre.astype(jnp.float32), axis=0)
    later_pre = from_behind(grad_pre, ("grp", "seq"), -2)
    tapped_signal = contract_cols(later_pre, w_taps[:width])
    nearby = cotangent.astype(jnp.float32) + contract_cols(grad_pre, w_taps[width:])
    grad_in = (nearby + tapped_signal).astype(jnp.bfloat16)
    seq_n = lax.axis_size("seq")
    grp_n = lax.axis_size("grp")
    chunks = seq_n * grp_n
    pair = part_bias.shape[0] // chunks
    used = part_taps.shape[1] + part_out.shape[1] + pair
    lanes = 128
    width = -(-used // lanes) * lanes
    packed = jnp.concatenate(
        [
            part_taps.reshape(chunks, -1),
            part_out.reshape(chunks, -1),
            part_bias.reshape(chunks, pair),
            jnp.zeros((chunks, width - used), jnp.float32),
        ],
        axis=1,
    )
    seq_bits = seq_n.bit_length() - 1
    grp_bits = grp_n.bit_length() - 1
    home = {}
    for b in range(seq_bits + grp_bits):
        home[b] = b + grp_bits if b < seq_bits else b - seq_bits
    core, x_hi, y1, y2, y4 = 0, 1, 2, 3, 4
    z1, z2, z4, x_lo = 5, 6, 7, 8
    orders = (
        [core, y1, z1, x_lo, y2, z2, x_hi, y4, z4],
        [core, z1, x_lo, y1, z2, y2, x_hi, z4, y4],
    )
    mine = halving_scatter(packed, ("grp", "seq"), orders, home)
    share = doubling_gather(mine, ("grp", "seq"), [z1, z2, z4, x_lo])
    taps_w = part_taps.shape[1]
    out_w = part_out.shape[1]
    grad_taps = share[:, :taps_w]
    grad_out = share[:, taps_w : taps_w + out_w]
    grad_bias = share[:, taps_w + out_w : used].reshape(-1)
    return (block_out, grad_in, grad_taps, grad_bias, grad_out)


def solution(mesh):
    placed = (P(("grp", "seq"), None), P(("grp", "seq"), None), P(), P(), P())
    return jax.shard_map(
        per_device,
        mesh=mesh,
        in_specs=placed,
        out_specs=(
            P(("grp", "seq"), None),
            P(("grp", "seq"), None),
            P("seq", None),
            P("seq"),
            P("seq", None),
        ),
        check_vma=False,
    )
```

```python
import jax
import jax.numpy as jnp
from jax import lax
from jax.sharding import PartitionSpec as P


def from_behind(array, axis, by):
    count = lax.axis_size(axis)
    pairs = [(i, i + by) for i in range(count) if 0 <= i + by < count]
    return lax.ppermute(array, axis, pairs)


def reduced_row_axes(left, right):
    return lax.dot_general(
        left, right, (((0,), (0,)), ((), ())), preferred_element_type=jnp.float32
    )


def contract_cols(left, right):
    return lax.dot_general(
        left, right, (((1,), (1,)), ((), ())), preferred_element_type=jnp.float32
    )


def relabel(index, rotate, size, by=1):
    ring = (index // rotate) % size
    return index + (((ring + by) % size) - ring) * rotate


def unlabel(index, rotate, size):
    return relabel(index, rotate, size, -1)


def halving_scatter(shares, axis, orders, ring):
    count = shares.shape[0]
    bits = count.bit_length() - 1
    rest = shares.shape[1:]
    rotate, size = ring
    where = lax.axis_index(axis)
    rows = []
    for c, order in enumerate(orders):
        for p in range(count // 2):
            v = c
            for t, b in enumerate(order[1:]):
                v |= ((p >> (bits - 2 - t)) & 1) << b
            rows.append(unlabel(v, rotate, size) if c else v)
    buf = jnp.concatenate([shares[s : s + 1] for s in rows])
    core = where & 1
    mine = jnp.where(core == 1, relabel(where, rotate, size), where)
    for step in range(bits):
        shift = [order[step] for order in orders]
        bit = jnp.where(core == 1, (mine >> shift[1]) & 1, (mine >> shift[0]) & 1)
        pairs = []
        for s in range(count):
            c = s & 1
            v = relabel(s, rotate, size) if c else s
            v ^= 1 << shift[c]
            pairs.append((s, unlabel(v, rotate, size) if c else v))
        split = buf.reshape((2, buf.shape[0] // 2) + rest)
        keep = lax.dynamic_index_in_dim(split, bit, 0, keepdims=False)
        send = lax.dynamic_index_in_dim(split, 1 - bit, 0, keepdims=False)
        buf = keep + lax.ppermute(send, axis, pairs)
    return buf[0]


def butterfly_sum(array, axes, orders, ring, inner):
    count = lax.axis_size(axes)
    rotate, size = ring
    for step in range(len(orders[0])):
        pairs = []
        for i in range(count):
            g, s = divmod(i, inner)
            c = s & 1
            v = relabel(g, rotate, size) if c else g
            v ^= 1 << orders[c][step]
            pairs.append((i, (unlabel(v, rotate, size) if c else v) * inner + s))
        array = array + lax.ppermute(array, axes, pairs)
    return array

def per_device(signal, cotangent, w_taps, gate_bias, w_out):
    width = signal.shape[1]
    units = w_out.shape[0]
    lagged_input = from_behind(signal, ("grp", "seq"), 2)
    preact = jnp.dot(signal, w_taps[width:], preferred_element_type=jnp.float32)
    preact = (
        preact
        + jnp.dot(lagged_input, w_taps[:width], preferred_element_type=jnp.float32)
        + gate_bias
    )
    squashed = jnp.tanh(preact[:, :units])
    opened = jax.nn.sigmoid(preact[:, units:])
    hidden_state = (squashed * opened).astype(jnp.bfloat16)
    block_out = (
        signal.astype(jnp.float32)
        + jnp.dot(hidden_state, w_out, preferred_element_type=jnp.float32)
    ).astype(jnp.bfloat16)
    grad_hidden = contract_cols(cotangent, w_out)
    grad_pre = jnp.concatenate(
        [
            grad_hidden * opened * (1.0 - squashed * squashed),
            grad_hidden * squashed * opened * (1.0 - opened),
        ],
        axis=1,
    ).astype(jnp.bfloat16)
    part_out = reduced_row_axes(hidden_state, cotangent)
    part_taps = jnp.concatenate(
        [reduced_row_axes(lagged_input, grad_pre), reduced_row_axes(signal, grad_pre)], axis=0
    )
    part_bias = jnp.sum(grad_pre.astype(jnp.float32), axis=0)
    later_pre = from_behind(grad_pre, ("grp", "seq"), -2)
    tapped_signal = contract_cols(later_pre, w_taps[:width])
    nearby = cotangent.astype(jnp.float32) + contract_cols(grad_pre, w_taps[width:])
    grad_in = (nearby + tapped_signal).astype(jnp.bfloat16)
    groups = lax.axis_size("seq")
    lanes = 128
    rows_taps = part_taps.shape[0] // groups
    rows_out = part_out.shape[0] // groups
    share_bias = part_bias.shape[0] // groups
    taps_r = rows_taps * part_taps.shape[1] // lanes
    out_r = rows_out * part_out.shape[1] // lanes
    bias_r = 8
    bias_rows = jnp.pad(part_bias.reshape(groups, 1, share_bias), ((0, 0), (0, bias_r), (0, lanes - share_bias)))[:, :bias_r]
    packed = jnp.concatenate(
        [
            part_taps.reshape(groups, taps_r, lanes),
            part_out.reshape(groups, out_r, lanes),
            bias_rows,
        ],
        axis=1,
    )
    mine = halving_scatter(packed, "seq", ([0, 2, 3, 1, 4], [0, 2, 1, 3, 4]), (4, 8))
    mine = butterfly_sum(mine, ("grp", "seq"), ([0, 3, 1, 2], [3, 0, 2, 1]), (1, 8), groups)
    grad_taps = mine[:taps_r].reshape(rows_taps, part_taps.shape[1])
    grad_out = mine[taps_r : taps_r + out_r].reshape(rows_out, part_out.shape[1])
    grad_bias = mine[taps_r + out_r, :share_bias]
    return (block_out, grad_in, grad_taps, grad_bias, grad_out)


def solution(mesh):
    placed = (P(("grp", "seq"), None), P(("grp", "seq"), None), P(), P(), P())
    return jax.shard_map(
        per_device,
        mesh=mesh,
        in_specs=placed,
        out_specs=(
            P(("grp", "seq"), None),
            P(("grp", "seq"), None),
            P("seq", None),
            P("seq"),
            P("seq", None),
        ),
        check_vma=False,
    )
```

```python
import jax
import jax.numpy as jnp
from jax import lax
from jax.sharding import PartitionSpec as P


def from_behind(array, axis, by):
    count = lax.axis_size(axis)
    pairs = [(i, i + by) for i in range(count) if 0 <= i + by < count]
    return lax.ppermute(array, axis, pairs)


def reduced_row_axes(left, right):
    return lax.dot_general(
        left, right, (((0,), (0,)), ((), ())), preferred_element_type=jnp.float32
    )


def contract_cols(left, right):
    return lax.dot_general(
        left, right, (((1,), (1,)), ((), ())), preferred_element_type=jnp.float32
    )


def relabel(index, rotate, size, by=1):
    ring = (index // rotate) % size
    return index + (((ring + by) % size) - ring) * rotate


def unlabel(index, rotate, size):
    return relabel(index, rotate, size, -1)


def halving_scatter(shares, axis, orders, ring):
    count = shares.shape[0]
    bits = count.bit_length() - 1
    rest = shares.shape[1:]
    rotate, size = ring
    where = lax.axis_index(axis)
    rows = []
    for c, order in enumerate(orders):
        for p in range(count // 2):
            v = c
            for t, b in enumerate(order[1:]):
                v |= ((p >> (bits - 2 - t)) & 1) << b
            rows.append(unlabel(v, rotate, size) if c else v)
    buf = jnp.concatenate([shares[s : s + 1] for s in rows])
    core = where & 1
    mine = jnp.where(core == 1, relabel(where, rotate, size), where)
    for step in range(bits):
        shift = [order[step] for order in orders]
        bit = jnp.where(core == 1, (mine >> shift[1]) & 1, (mine >> shift[0]) & 1)
        pairs = []
        for s in range(count):
            c = s & 1
            v = relabel(s, rotate, size) if c else s
            v ^= 1 << shift[c]
            pairs.append((s, unlabel(v, rotate, size) if c else v))
        split = buf.reshape((2, buf.shape[0] // 2) + rest)
        keep = lax.dynamic_index_in_dim(split, bit, 0, keepdims=False)
        send = lax.dynamic_index_in_dim(split, 1 - bit, 0, keepdims=False)
        buf = keep + lax.ppermute(send, axis, pairs)
    return buf[0]


def butterfly_sum(array, axes, orders, ring, inner):
    count = lax.axis_size(axes)
    rotate, size = ring
    for step in range(len(orders[0])):
        pairs = []
        for i in range(count):
            g, s = divmod(i, inner)
            c = s & 1
            v = relabel(g, rotate, size) if c else g
            v ^= 1 << orders[c][step]
            pairs.append((i, (unlabel(v, rotate, size) if c else v) * inner + s))
        array = array + lax.ppermute(array, axes, pairs)
    return array

def quad_sum(array, axis, pairs):
    count = lax.axis_size(axis)
    where = lax.axis_index(axis)
    for lo, hi in pairs:
        masks = [1 << lo, 1 << hi, (1 << lo) | (1 << hi)]
        got = [lax.ppermute(array, axis, [(i, i ^ m) for i in range(count)]) for m in masks]
        q = ((where >> lo) & 1) + 2 * ((where >> hi) & 1)
        by_mask = [array] + got
        vals = []
        for k in range(4):
            x = k ^ q
            v = jnp.where(x == 1, by_mask[1], by_mask[0])
            v = jnp.where(x == 2, by_mask[2], v)
            vals.append(jnp.where(x == 3, by_mask[3], v))
        array = (vals[0] + vals[1]) + (vals[2] + vals[3])
    return array


def per_device(signal, cotangent, w_taps, gate_bias, w_out):
    width = signal.shape[1]
    units = w_out.shape[0]
    lagged_input = from_behind(signal, ("grp", "seq"), 2)
    preact = jnp.dot(signal, w_taps[width:], preferred_element_type=jnp.float32)
    preact = (
        preact
        + jnp.dot(lagged_input, w_taps[:width], preferred_element_type=jnp.float32)
        + gate_bias
    )
    squashed = jnp.tanh(preact[:, :units])
    opened = jax.nn.sigmoid(preact[:, units:])
    hidden_state = (squashed * opened).astype(jnp.bfloat16)
    block_out = (
        signal.astype(jnp.float32)
        + jnp.dot(hidden_state, w_out, preferred_element_type=jnp.float32)
    ).astype(jnp.bfloat16)
    grad_hidden = contract_cols(cotangent, w_out)
    grad_pre = jnp.concatenate(
        [
            grad_hidden * opened * (1.0 - squashed * squashed),
            grad_hidden * squashed * opened * (1.0 - opened),
        ],
        axis=1,
    ).astype(jnp.bfloat16)
    part_out = reduced_row_axes(hidden_state, cotangent)
    part_taps = jnp.concatenate(
        [reduced_row_axes(lagged_input, grad_pre), reduced_row_axes(signal, grad_pre)], axis=0
    )
    part_bias = jnp.sum(grad_pre.astype(jnp.float32), axis=0)
    later_pre = from_behind(grad_pre, ("grp", "seq"), -2)
    tapped_signal = contract_cols(later_pre, w_taps[:width])
    nearby = cotangent.astype(jnp.float32) + contract_cols(grad_pre, w_taps[width:])
    grad_in = (nearby + tapped_signal).astype(jnp.bfloat16)
    groups = lax.axis_size("seq")
    lanes = 128
    rows_taps = part_taps.shape[0] // groups
    rows_out = part_out.shape[0] // groups
    share_bias = part_bias.shape[0] // groups
    taps_r = rows_taps * part_taps.shape[1] // lanes
    out_r = rows_out * part_out.shape[1] // lanes
    bias_r = 8
    bias_rows = jnp.pad(part_bias.reshape(groups, 1, share_bias), ((0, 0), (0, bias_r), (0, lanes - share_bias)))[:, :bias_r]
    packed = jnp.concatenate(
        [
            part_taps.reshape(groups, taps_r, lanes),
            part_out.reshape(groups, out_r, lanes),
            bias_rows,
        ],
        axis=1,
    )
    mine = halving_scatter(packed, "seq", ([0, 2, 3, 1, 4], [0, 2, 1, 3, 4]), (4, 8))
    mine = quad_sum(mine, "grp", [(0, 3), (1, 2)])
    grad_taps = mine[:taps_r].reshape(rows_taps, part_taps.shape[1])
    grad_out = mine[taps_r : taps_r + out_r].reshape(rows_out, part_out.shape[1])
    grad_bias = mine[taps_r + out_r, :share_bias]
    return (block_out, grad_in, grad_taps, grad_bias, grad_out)


def solution(mesh):
    placed = (P(("grp", "seq"), None), P(("grp", "seq"), None), P(), P(), P())
    return jax.shard_map(
        per_device,
        mesh=mesh,
        in_specs=placed,
        out_specs=(
            P(("grp", "seq"), None),
            P(("grp", "seq"), None),
            P("seq", None),
            P("seq"),
            P("seq", None),
        ),
        check_vma=False,
    )
```

```python
import jax
import jax.numpy as jnp
from jax import lax
from jax.sharding import PartitionSpec as P


def from_behind(array, axis, by):
    count = lax.axis_size(axis)
    pairs = [(i, i + by) for i in range(count) if 0 <= i + by < count]
    return lax.ppermute(array, axis, pairs)


def reduced_row_axes(left, right):
    return lax.dot_general(
        left, right, (((0,), (0,)), ((), ())), preferred_element_type=jnp.float32
    )


def contract_cols(left, right):
    return lax.dot_general(
        left, right, (((1,), (1,)), ((), ())), preferred_element_type=jnp.float32
    )


def relabel(index, rotate, size, by=1):
    ring = (index // rotate) % size
    return index + (((ring + by) % size) - ring) * rotate


def unlabel(index, rotate, size):
    return relabel(index, rotate, size, -1)


def share_rows(count, orders, ring):
    bits = count.bit_length() - 1
    rotate, size = ring
    rows = []
    for c, order in enumerate(orders):
        for p in range(count // 2):
            v = c
            for t, b in enumerate(order[1:]):
                v |= ((p >> (bits - 2 - t)) & 1) << b
            rows.append(unlabel(v, rotate, size) if c else v)
    return rows


def halving_scatter(shares, axis, orders, ring):
    count = shares.shape[0]
    bits = count.bit_length() - 1
    rest = shares.shape[1:]
    rotate, size = ring
    where = lax.axis_index(axis)
    buf = shares
    core = where & 1
    mine = jnp.where(core == 1, relabel(where, rotate, size), where)
    for step in range(bits):
        shift = [order[step] for order in orders]
        bit = jnp.where(core == 1, (mine >> shift[1]) & 1, (mine >> shift[0]) & 1)
        pairs = []
        for s in range(count):
            c = s & 1
            v = relabel(s, rotate, size) if c else s
            v ^= 1 << shift[c]
            pairs.append((s, unlabel(v, rotate, size) if c else v))
        split = buf.reshape((2, buf.shape[0] // 2) + rest)
        keep = lax.dynamic_index_in_dim(split, bit, 0, keepdims=False)
        send = lax.dynamic_index_in_dim(split, 1 - bit, 0, keepdims=False)
        buf = keep + lax.ppermute(send, axis, pairs)
    return buf[0]


def butterfly_sum(array, axes, orders, ring, inner):
    count = lax.axis_size(axes)
    rotate, size = ring
    for step in range(len(orders[0])):
        pairs = []
        for i in range(count):
            g, s = divmod(i, inner)
            c = s & 1
            v = relabel(g, rotate, size) if c else g
            v ^= 1 << orders[c][step]
            pairs.append((i, (unlabel(v, rotate, size) if c else v) * inner + s))
        array = array + lax.ppermute(array, axes, pairs)
    return array

def per_device(signal, cotangent, w_taps, gate_bias, w_out):
    width = signal.shape[1]
    units = w_out.shape[0]
    lagged_input = from_behind(signal, ("grp", "seq"), 2)
    preact = jnp.dot(signal, w_taps[width:], preferred_element_type=jnp.float32)
    preact = (
        preact
        + jnp.dot(lagged_input, w_taps[:width], preferred_element_type=jnp.float32)
        + gate_bias
    )
    squashed = jnp.tanh(preact[:, :units])
    opened = jax.nn.sigmoid(preact[:, units:])
    hidden_state = (squashed * opened).astype(jnp.bfloat16)
    block_out = (
        signal.astype(jnp.float32)
        + jnp.dot(hidden_state, w_out, preferred_element_type=jnp.float32)
    ).astype(jnp.bfloat16)
    grad_hidden = contract_cols(cotangent, w_out)
    grad_pre = jnp.concatenate(
        [
            grad_hidden * opened * (1.0 - squashed * squashed),
            grad_hidden * squashed * opened * (1.0 - opened),
        ],
        axis=1,
    ).astype(jnp.bfloat16)
    groups = lax.axis_size("seq")
    orders = ([0, 2, 3, 1, 4], [0, 2, 1, 3, 4])
    ring = (4, 8)
    rows = share_rows(groups, orders, ring)

    def in_share_order(array):
        step = array.shape[1] // groups
        return jnp.concatenate([array[:, s * step : (s + 1) * step] for s in rows], axis=1)

    part_out = reduced_row_axes(in_share_order(hidden_state), cotangent)
    inputs = jnp.concatenate([lagged_input, signal], axis=1)
    part_taps = reduced_row_axes(in_share_order(inputs), grad_pre)
    part_bias = jnp.sum(grad_pre.astype(jnp.float32), axis=0)
    part_bias = in_share_order(part_bias[None])[0]
    later_pre = from_behind(grad_pre, ("grp", "seq"), -2)
    tapped_signal = contract_cols(later_pre, w_taps[:width])
    nearby = cotangent.astype(jnp.float32) + contract_cols(grad_pre, w_taps[width:])
    grad_in = (nearby + tapped_signal).astype(jnp.bfloat16)
    lanes = 128
    rows_taps = part_taps.shape[0] // groups
    rows_out = part_out.shape[0] // groups
    share_bias = part_bias.shape[0] // groups
    taps_r = rows_taps * part_taps.shape[1] // lanes
    out_r = rows_out * part_out.shape[1] // lanes
    bias_r = 8
    bias_rows = jnp.pad(part_bias.reshape(groups, 1, share_bias), ((0, 0), (0, bias_r), (0, lanes - share_bias)))[:, :bias_r]
    packed = jnp.concatenate(
        [
            part_taps.reshape(groups, taps_r, lanes),
            part_out.reshape(groups, out_r, lanes),
            bias_rows,
        ],
        axis=1,
    )
    mine = halving_scatter(packed, "seq", orders, ring)
    mine = butterfly_sum(mine, ("grp", "seq"), ([0, 3, 1, 2], [3, 0, 2, 1]), (1, 8), groups)
    grad_taps = mine[:taps_r].reshape(rows_taps, part_taps.shape[1])
    grad_out = mine[taps_r : taps_r + out_r].reshape(rows_out, part_out.shape[1])
    grad_bias = mine[taps_r + out_r, :share_bias]
    return (block_out, grad_in, grad_taps, grad_bias, grad_out)


def solution(mesh):
    placed = (P(("grp", "seq"), None), P(("grp", "seq"), None), P(), P(), P())
    return jax.shard_map(
        per_device,
        mesh=mesh,
        in_specs=placed,
        out_specs=(
            P(("grp", "seq"), None),
            P(("grp", "seq"), None),
            P("seq", None),
            P("seq"),
            P("seq", None),
        ),
        check_vma=False,
    )
```

```python
import jax
import jax.numpy as jnp
from jax import lax
from jax.sharding import PartitionSpec as P


def from_behind(array, axis, by):
    count = lax.axis_size(axis)
    pairs = [(i, i + by) for i in range(count) if 0 <= i + by < count]
    return lax.ppermute(array, axis, pairs)


def reduced_row_axes(left, right):
    return lax.dot_general(
        left, right, (((0,), (0,)), ((), ())), preferred_element_type=jnp.float32
    )


def contract_cols(left, right):
    return lax.dot_general(
        left, right, (((1,), (1,)), ((), ())), preferred_element_type=jnp.float32
    )


def relabel(index, rotate, size, by=1):
    ring = (index // rotate) % size
    return index + (((ring + by) % size) - ring) * rotate


def unlabel(index, rotate, size):
    return relabel(index, rotate, size, -1)


def halving_scatter(shares, axis, orders, ring):
    count = shares.shape[0]
    bits = count.bit_length() - 1
    rest = shares.shape[1:]
    rotate, size = ring
    where = lax.axis_index(axis)
    rows = []
    for c, order in enumerate(orders):
        for p in range(count // 2):
            v = c
            for t, b in enumerate(order[1:]):
                v |= ((p >> (bits - 2 - t)) & 1) << b
            rows.append(unlabel(v, rotate, size) if c else v)
    buf = jnp.concatenate([shares[s : s + 1] for s in rows])
    core = where & 1
    mine = jnp.where(core == 1, relabel(where, rotate, size), where)
    for step in range(bits):
        shift = [order[step] for order in orders]
        bit = jnp.where(core == 1, (mine >> shift[1]) & 1, (mine >> shift[0]) & 1)
        pairs = []
        for s in range(count):
            c = s & 1
            v = relabel(s, rotate, size) if c else s
            v ^= 1 << shift[c]
            pairs.append((s, unlabel(v, rotate, size) if c else v))
        split = buf.reshape((2, buf.shape[0] // 2) + rest)
        keep = lax.dynamic_index_in_dim(split, bit, 0, keepdims=False)
        send = lax.dynamic_index_in_dim(split, 1 - bit, 0, keepdims=False)
        buf = keep + lax.ppermute(send, axis, pairs)
    return buf[0]


def butterfly_sum(array, axes, orders, ring, inner):
    count = lax.axis_size(axes)
    rotate, size = ring
    for step in range(len(orders[0])):
        pairs = []
        for i in range(count):
            g, s = divmod(i, inner)
            c = s & 1
            v = relabel(g, rotate, size) if c else g
            v ^= 1 << orders[c][step]
            pairs.append((i, (unlabel(v, rotate, size) if c else v) * inner + s))
        array = array + lax.ppermute(array, axes, pairs)
    return array

def per_device(signal, cotangent, w_taps, gate_bias, w_out):
    width = signal.shape[1]
    units = w_out.shape[0]
    lagged_input = from_behind(signal, ("grp", "seq"), 2)
    preact = jnp.dot(signal, w_taps[width:], preferred_element_type=jnp.float32)
    preact = (
        preact
        + jnp.dot(lagged_input, w_taps[:width], preferred_element_type=jnp.float32)
        + gate_bias
    )
    squashed = jnp.tanh(preact[:, :units])
    opened = jax.nn.sigmoid(preact[:, units:])
    hidden_state = (squashed * opened).astype(jnp.bfloat16)
    block_out = (
        signal.astype(jnp.float32)
        + jnp.dot(hidden_state, w_out, preferred_element_type=jnp.float32)
    ).astype(jnp.bfloat16)
    grad_hidden = contract_cols(cotangent, w_out)
    grad_pre = jnp.concatenate(
        [
            grad_hidden * opened * (1.0 - squashed * squashed),
            grad_hidden * squashed * opened * (1.0 - opened),
        ],
        axis=1,
    ).astype(jnp.bfloat16)
    part_out = reduced_row_axes(hidden_state, cotangent)
    part_taps = jnp.concatenate(
        [reduced_row_axes(lagged_input, grad_pre), reduced_row_axes(signal, grad_pre)], axis=0
    )
    part_bias = jnp.sum(grad_pre.astype(jnp.float32), axis=0)
    later_pre = from_behind(grad_pre, ("grp", "seq"), -2)
    groups = lax.axis_size("seq")
    lanes = 128
    rows_taps = part_taps.shape[0] // groups
    rows_out = part_out.shape[0] // groups
    share_bias = part_bias.shape[0] // groups
    taps_r = rows_taps * part_taps.shape[1] // lanes
    out_r = rows_out * part_out.shape[1] // lanes
    bias_r = 8
    bias_rows = jnp.pad(part_bias.reshape(groups, 1, share_bias), ((0, 0), (0, bias_r), (0, lanes - share_bias)))[:, :bias_r]
    packed = jnp.concatenate(
        [
            part_taps.reshape(groups, taps_r, lanes),
            part_out.reshape(groups, out_r, lanes),
            bias_rows,
        ],
        axis=1,
    )
    later_pre, packed = lax.optimization_barrier((later_pre, packed))
    tapped_signal = contract_cols(later_pre, w_taps[:width])
    nearby = cotangent.astype(jnp.float32) + contract_cols(grad_pre, w_taps[width:])
    grad_in = (nearby + tapped_signal).astype(jnp.bfloat16)
    mine = halving_scatter(packed, "seq", ([0, 2, 3, 1, 4], [0, 2, 1, 3, 4]), (4, 8))
    mine = butterfly_sum(mine, ("grp", "seq"), ([0, 3, 1, 2], [3, 0, 2, 1]), (1, 8), groups)
    grad_taps = mine[:taps_r].reshape(rows_taps, part_taps.shape[1])
    grad_out = mine[taps_r : taps_r + out_r].reshape(rows_out, part_out.shape[1])
    grad_bias = mine[taps_r + out_r, :share_bias]
    return (block_out, grad_in, grad_taps, grad_bias, grad_out)


def solution(mesh):
    placed = (P(("grp", "seq"), None), P(("grp", "seq"), None), P(), P(), P())
    return jax.shard_map(
        per_device,
        mesh=mesh,
        in_specs=placed,
        out_specs=(
            P(("grp", "seq"), None),
            P(("grp", "seq"), None),
            P("seq", None),
            P("seq"),
            P("seq", None),
        ),
        check_vma=False,
    )
```

```python
import jax
import jax.numpy as jnp
from jax import lax
from jax.sharding import PartitionSpec as P


def from_behind(array, axis, by):
    count = lax.axis_size(axis)
    pairs = [(i, i + by) for i in range(count) if 0 <= i + by < count]
    return lax.ppermute(array, axis, pairs)


def reduced_row_axes(left, right):
    return lax.dot_general(
        left, right, (((0,), (0,)), ((), ())), preferred_element_type=jnp.float32
    )


def contract_cols(left, right):
    return lax.dot_general(
        left, right, (((1,), (1,)), ((), ())), preferred_element_type=jnp.float32
    )


def relabel(index, rotate, size, by=1):
    ring = (index // rotate) % size
    return index + (((ring + by) % size) - ring) * rotate


def unlabel(index, rotate, size):
    return relabel(index, rotate, size, -1)


def halving_scatter(shares, axis, orders, ring):
    count = shares.shape[0]
    bits = count.bit_length() - 1
    rest = shares.shape[1:]
    rotate, size = ring
    where = lax.axis_index(axis)
    rows = []
    for c, order in enumerate(orders):
        for p in range(count // 2):
            v = c
            for t, b in enumerate(order[1:]):
                v |= ((p >> (bits - 2 - t)) & 1) << b
            rows.append(unlabel(v, rotate, size) if c else v)
    buf = jnp.take(shares, jnp.array(rows, jnp.int32), axis=0)
    core = where & 1
    mine = jnp.where(core == 1, relabel(where, rotate, size), where)
    for step in range(bits):
        shift = [order[step] for order in orders]
        bit = jnp.where(core == 1, (mine >> shift[1]) & 1, (mine >> shift[0]) & 1)
        pairs = []
        for s in range(count):
            c = s & 1
            v = relabel(s, rotate, size) if c else s
            v ^= 1 << shift[c]
            pairs.append((s, unlabel(v, rotate, size) if c else v))
        split = buf.reshape((2, buf.shape[0] // 2) + rest)
        keep = lax.dynamic_index_in_dim(split, bit, 0, keepdims=False)
        send = lax.dynamic_index_in_dim(split, 1 - bit, 0, keepdims=False)
        buf = keep + lax.ppermute(send, axis, pairs)
    return buf[0]


def butterfly_sum(array, axes, orders, ring, inner):
    count = lax.axis_size(axes)
    rotate, size = ring
    for step in range(len(orders[0])):
        pairs = []
        for i in range(count):
            g, s = divmod(i, inner)
            c = s & 1
            v = relabel(g, rotate, size) if c else g
            v ^= 1 << orders[c][step]
            pairs.append((i, (unlabel(v, rotate, size) if c else v) * inner + s))
        array = array + lax.ppermute(array, axes, pairs)
    return array

def per_device(signal, cotangent, w_taps, gate_bias, w_out):
    width = signal.shape[1]
    units = w_out.shape[0]
    lagged_input = from_behind(signal, ("grp", "seq"), 2)
    preact = jnp.dot(signal, w_taps[width:], preferred_element_type=jnp.float32)
    preact = (
        preact
        + jnp.dot(lagged_input, w_taps[:width], preferred_element_type=jnp.float32)
        + gate_bias
    )
    squashed = jnp.tanh(preact[:, :units])
    opened = jax.nn.sigmoid(preact[:, units:])
    hidden_state = (squashed * opened).astype(jnp.bfloat16)
    block_out = (
        signal.astype(jnp.float32)
        + jnp.dot(hidden_state, w_out, preferred_element_type=jnp.float32)
    ).astype(jnp.bfloat16)
    grad_hidden = contract_cols(cotangent, w_out)
    grad_pre = jnp.concatenate(
        [
            grad_hidden * opened * (1.0 - squashed * squashed),
            grad_hidden * squashed * opened * (1.0 - opened),
        ],
        axis=1,
    ).astype(jnp.bfloat16)
    part_out = reduced_row_axes(hidden_state, cotangent)
    part_taps = jnp.concatenate(
        [reduced_row_axes(lagged_input, grad_pre), reduced_row_axes(signal, grad_pre)], axis=0
    )
    part_bias = jnp.sum(grad_pre.astype(jnp.float32), axis=0)
    later_pre = from_behind(grad_pre, ("grp", "seq"), -2)
    tapped_signal = contract_cols(later_pre, w_taps[:width])
    nearby = cotangent.astype(jnp.float32) + contract_cols(grad_pre, w_taps[width:])
    grad_in = (nearby + tapped_signal).astype(jnp.bfloat16)
    groups = lax.axis_size("seq")
    lanes = 128
    rows_taps = part_taps.shape[0] // groups
    rows_out = part_out.shape[0] // groups
    share_bias = part_bias.shape[0] // groups
    taps_r = rows_taps * part_taps.shape[1] // lanes
    out_r = rows_out * part_out.shape[1] // lanes
    bias_r = 8
    bias_rows = jnp.pad(part_bias.reshape(groups, 1, share_bias), ((0, 0), (0, bias_r), (0, lanes - share_bias)))[:, :bias_r]
    packed = jnp.concatenate(
        [
            part_taps.reshape(groups, taps_r, lanes),
            part_out.reshape(groups, out_r, lanes),
            bias_rows,
        ],
        axis=1,
    )
    mine = halving_scatter(packed, "seq", ([0, 2, 3, 1, 4], [0, 2, 1, 3, 4]), (4, 8))
    mine = butterfly_sum(mine, ("grp", "seq"), ([0, 3, 1, 2], [3, 0, 2, 1]), (1, 8), groups)
    grad_taps = mine[:taps_r].reshape(rows_taps, part_taps.shape[1])
    grad_out = mine[taps_r : taps_r + out_r].reshape(rows_out, part_out.shape[1])
    grad_bias = mine[taps_r + out_r, :share_bias]
    return (block_out, grad_in, grad_taps, grad_bias, grad_out)


def solution(mesh):
    placed = (P(("grp", "seq"), None), P(("grp", "seq"), None), P(), P(), P())
    return jax.shard_map(
        per_device,
        mesh=mesh,
        in_specs=placed,
        out_specs=(
            P(("grp", "seq"), None),
            P(("grp", "seq"), None),
            P("seq", None),
            P("seq"),
            P("seq", None),
        ),
        check_vma=False,
    )
```

```python
import jax
import jax.numpy as jnp
from jax import lax
from jax.sharding import PartitionSpec as P


def from_behind(array, axis, by):
    count = lax.axis_size(axis)
    pairs = [(i, i + by) for i in range(count) if 0 <= i + by < count]
    return lax.ppermute(array, axis, pairs)


def reduced_row_axes(left, right):
    return lax.dot_general(
        left, right, (((0,), (0,)), ((), ())), preferred_element_type=jnp.float32
    )


def contract_cols(left, right):
    return lax.dot_general(
        left, right, (((1,), (1,)), ((), ())), preferred_element_type=jnp.float32
    )


def relabel(index, rotate, size, by=1):
    ring = (index // rotate) % size
    return index + (((ring + by) % size) - ring) * rotate


def unlabel(index, rotate, size):
    return relabel(index, rotate, size, -1)


def halving_scatter(shares, axis, orders, ring):
    count = shares.shape[0]
    bits = count.bit_length() - 1
    rest = shares.shape[1:]
    rotate, size = ring
    where = lax.axis_index(axis)
    rows = []
    for c, order in enumerate(orders):
        for p in range(count // 2):
            v = c
            for t, b in enumerate(order[1:]):
                v |= ((p >> (bits - 2 - t)) & 1) << b
            rows.append(unlabel(v, rotate, size) if c else v)
    buf = jnp.concatenate([shares[s : s + 1] for s in rows])
    core = where & 1
    mine = jnp.where(core == 1, relabel(where, rotate, size), where)
    for step in range(bits):
        shift = [order[step] for order in orders]
        bit = jnp.where(core == 1, (mine >> shift[1]) & 1, (mine >> shift[0]) & 1)
        pairs = []
        for s in range(count):
            c = s & 1
            v = relabel(s, rotate, size) if c else s
            v ^= 1 << shift[c]
            pairs.append((s, unlabel(v, rotate, size) if c else v))
        split = buf.reshape((2, buf.shape[0] // 2) + rest)
        keep = lax.dynamic_index_in_dim(split, bit, 0, keepdims=False)
        send = lax.dynamic_index_in_dim(split, 1 - bit, 0, keepdims=False)
        buf = keep + lax.ppermute(send, axis, pairs)
    return buf[0]


def butterfly_sum(array, axes, orders, ring, inner):
    count = lax.axis_size(axes)
    rotate, size = ring
    for step in range(len(orders[0])):
        pairs = []
        for i in range(count):
            g, s = divmod(i, inner)
            c = s & 1
            v = relabel(g, rotate, size) if c else g
            v ^= 1 << orders[c][step]
            pairs.append((i, (unlabel(v, rotate, size) if c else v) * inner + s))
        array = array + lax.ppermute(array, axes, pairs)
    return array

def per_device(signal, cotangent, w_taps, gate_bias, w_out):
    width = signal.shape[1]
    units = w_out.shape[0]
    lagged_input = from_behind(signal, ("grp", "seq"), 2)
    preact = jnp.dot(signal, w_taps[width:], preferred_element_type=jnp.float32)
    preact = (
        preact
        + jnp.dot(lagged_input, w_taps[:width], preferred_element_type=jnp.float32)
        + gate_bias
    )
    squashed = jnp.tanh(preact[:, :units])
    opened = jax.nn.sigmoid(preact[:, units:])
    hidden_state = (squashed * opened).astype(jnp.bfloat16)
    block_out = (
        signal.astype(jnp.float32)
        + jnp.dot(hidden_state, w_out, preferred_element_type=jnp.float32)
    ).astype(jnp.bfloat16)
    grad_hidden = contract_cols(cotangent, w_out)
    grad_pre = jnp.concatenate(
        [
            grad_hidden * opened * (1.0 - squashed * squashed),
            grad_hidden * squashed * opened * (1.0 - opened),
        ],
        axis=1,
    ).astype(jnp.bfloat16)
    part_out = reduced_row_axes(hidden_state, cotangent)
    part_taps = jnp.concatenate(
        [reduced_row_axes(lagged_input, grad_pre), reduced_row_axes(signal, grad_pre)], axis=0
    )
    part_bias = jnp.sum(grad_pre.astype(jnp.float32), axis=0)
    later_pre = from_behind(grad_pre, ("grp", "seq"), -2)
    tapped_signal = contract_cols(later_pre, w_taps[:width])
    nearby = cotangent.astype(jnp.float32) + contract_cols(grad_pre, w_taps[width:])
    grad_in = (nearby + tapped_signal).astype(jnp.bfloat16)
    groups = lax.axis_size("seq")
    lanes = 128
    rows_taps = part_taps.shape[0] // groups
    rows_out = part_out.shape[0] // groups
    share_bias = part_bias.shape[0] // groups
    taps_r = rows_taps * part_taps.shape[1] // lanes
    out_r = rows_out * part_out.shape[1] // lanes
    bias_r = 8
    bias_rows = jnp.pad(part_bias.reshape(groups, 1, share_bias), ((0, 0), (0, bias_r), (0, lanes - share_bias)))[:, :bias_r]
    packed = jnp.concatenate(
        [
            part_taps.reshape(groups, taps_r, lanes),
            part_out.reshape(groups, out_r, lanes),
            bias_rows,
        ],
        axis=1,
    )
    mine = halving_scatter(packed, "seq", ([0, 2, 3, 1, 4], [0, 2, 1, 3, 4]), (4, 8))
    mine = butterfly_sum(mine, ("grp", "seq"), ([0, 1, 2, 3], [3, 0, 1, 2]), (1, 8), groups)
    grad_taps = mine[:taps_r].reshape(rows_taps, part_taps.shape[1])
    grad_out = mine[taps_r : taps_r + out_r].reshape(rows_out, part_out.shape[1])
    grad_bias = mine[taps_r + out_r, :share_bias]
    return (block_out, grad_in, grad_taps, grad_bias, grad_out)


def solution(mesh):
    placed = (P(("grp", "seq"), None), P(("grp", "seq"), None), P(), P(), P())
    return jax.shard_map(
        per_device,
        mesh=mesh,
        in_specs=placed,
        out_specs=(
            P(("grp", "seq"), None),
            P(("grp", "seq"), None),
            P("seq", None),
            P("seq"),
            P("seq", None),
        ),
        check_vma=False,
    )
```

```python
import jax
import jax.numpy as jnp
from jax import lax
from jax.sharding import PartitionSpec as P


def from_behind(array, axis, by):
    count = lax.axis_size(axis)
    pairs = [(i, i + by) for i in range(count) if 0 <= i + by < count]
    return lax.ppermute(array, axis, pairs)


def reduced_row_axes(left, right):
    return lax.dot_general(
        left, right, (((0,), (0,)), ((), ())), preferred_element_type=jnp.float32
    )


def contract_cols(left, right):
    return lax.dot_general(
        left, right, (((1,), (1,)), ((), ())), preferred_element_type=jnp.float32
    )


def relabel(index, rotate, size, by=1):
    ring = (index // rotate) % size
    return index + (((ring + by) % size) - ring) * rotate


def unlabel(index, rotate, size):
    return relabel(index, rotate, size, -1)


def halving_scatter(shares, axis, orders, ring):
    count = shares.shape[0]
    bits = count.bit_length() - 1
    rest = shares.shape[1:]
    rotate, size = ring
    where = lax.axis_index(axis)
    rows = []
    for c, order in enumerate(orders):
        for p in range(count // 2):
            v = c
            for t, b in enumerate(order[1:]):
                v |= ((p >> (bits - 2 - t)) & 1) << b
            rows.append(unlabel(v, rotate, size) if c else v)
    buf = jnp.concatenate([shares[s : s + 1] for s in rows])
    core = where & 1
    mine = jnp.where(core == 1, relabel(where, rotate, size), where)
    for step in range(bits):
        shift = [order[step] for order in orders]
        bit = jnp.where(core == 1, (mine >> shift[1]) & 1, (mine >> shift[0]) & 1)
        pairs = []
        for s in range(count):
            c = s & 1
            v = relabel(s, rotate, size) if c else s
            v ^= 1 << shift[c]
            pairs.append((s, unlabel(v, rotate, size) if c else v))
        split = buf.reshape((2, buf.shape[0] // 2) + rest)
        keep = lax.dynamic_index_in_dim(split, bit, 0, keepdims=False)
        send = lax.dynamic_index_in_dim(split, 1 - bit, 0, keepdims=False)
        buf = keep + lax.ppermute(send, axis, pairs)
    return buf[0]


def butterfly_sum(array, axes, orders, ring, inner):
    count = lax.axis_size(axes)
    rotate, size = ring
    for step in range(len(orders[0])):
        pairs = []
        for i in range(count):
            g, s = divmod(i, inner)
            c = s & 1
            v = relabel(g, rotate, size) if c else g
            v ^= 1 << orders[c][step]
            pairs.append((i, (unlabel(v, rotate, size) if c else v) * inner + s))
        array = array + lax.ppermute(array, axes, pairs)
    return array

def per_device(signal, cotangent, w_taps, gate_bias, w_out):
    width = signal.shape[1]
    units = w_out.shape[0]
    lagged_input = from_behind(signal, ("grp", "seq"), 2)
    preact = jnp.dot(signal, w_taps[width:], preferred_element_type=jnp.float32)
    preact = (
        preact
        + jnp.dot(lagged_input, w_taps[:width], preferred_element_type=jnp.float32)
        + gate_bias
    )
    squashed = jnp.tanh(preact[:, :units])
    opened = jax.nn.sigmoid(preact[:, units:])
    hidden_state = (squashed * opened).astype(jnp.bfloat16)
    block_out = (
        signal.astype(jnp.float32)
        + jnp.dot(hidden_state, w_out, preferred_element_type=jnp.float32)
    ).astype(jnp.bfloat16)
    grad_hidden = contract_cols(cotangent, w_out)
    grad_pre = jnp.concatenate(
        [
            grad_hidden * opened * (1.0 - squashed * squashed),
            grad_hidden * squashed * opened * (1.0 - opened),
        ],
        axis=1,
    ).astype(jnp.bfloat16)
    part_out = reduced_row_axes(hidden_state, cotangent)
    part_taps = jnp.concatenate(
        [reduced_row_axes(lagged_input, grad_pre), reduced_row_axes(signal, grad_pre)], axis=0
    )
    part_bias = jnp.sum(grad_pre.astype(jnp.float32), axis=0)
    later_pre = from_behind(grad_pre, ("grp", "seq"), -2)
    tapped_signal = contract_cols(later_pre, w_taps[:width])
    nearby = cotangent.astype(jnp.float32) + contract_cols(grad_pre, w_taps[width:])
    grad_in = (nearby + tapped_signal).astype(jnp.bfloat16)
    groups = lax.axis_size("seq")
    lanes = 128
    rows_taps = part_taps.shape[0] // groups
    rows_out = part_out.shape[0] // groups
    share_bias = part_bias.shape[0] // groups
    taps_r = rows_taps * part_taps.shape[1] // lanes
    out_r = rows_out * part_out.shape[1] // lanes
    bias_r = 8
    bias_rows = jnp.pad(part_bias.reshape(groups, 1, share_bias), ((0, 0), (0, bias_r), (0, lanes - share_bias)))[:, :bias_r]
    packed = jnp.concatenate(
        [
            part_taps.reshape(groups, taps_r, lanes),
            part_out.reshape(groups, out_r, lanes),
            bias_rows,
        ],
        axis=1,
    )
    mine = halving_scatter(packed, "seq", ([0, 2, 3, 1, 4], [0, 2, 1, 3, 4]), (4, 8))
    mine = butterfly_sum(mine, ("grp", "seq"), ([0, 1, 2, 3], [2, 3, 0, 1]), (1, 8), groups)
    grad_taps = mine[:taps_r].reshape(rows_taps, part_taps.shape[1])
    grad_out = mine[taps_r : taps_r + out_r].reshape(rows_out, part_out.shape[1])
    grad_bias = mine[taps_r + out_r, :share_bias]
    return (block_out, grad_in, grad_taps, grad_bias, grad_out)


def solution(mesh):
    placed = (P(("grp", "seq"), None), P(("grp", "seq"), None), P(), P(), P())
    return jax.shard_map(
        per_device,
        mesh=mesh,
        in_specs=placed,
        out_specs=(
            P(("grp", "seq"), None),
            P(("grp", "seq"), None),
            P("seq", None),
            P("seq"),
            P("seq", None),
        ),
        check_vma=False,
    )
```
